128 devices in a mesh: dp: 16 (over z, x), tensor: 4 (over y), section: 2 (over core).
Axes of the slice: x: 4, y: 4, z: 4, core: 2. Of those that a mesh axis runs over, the one named last changes fastest.
Arguments:
- grad_mat: bfloat16 [16, 4, 1600, 4800], P('dp', 'tensor', 'section'), may hold values from -6 to 6
- grad_vec: bfloat16 [16, 20800], P('dp'), may hold values from -6 to 6
- master_mat: float32 [4, 2, 16, 50, 4800], P('tensor', 'section', 'dp'), may hold values from -9 to 9
- first_mat: float32 [4, 2, 16, 50, 4800], P('tensor', 'section', 'dp'), may hold values from -4 to 4
- second_mat: float32 [4, 2, 16, 50, 4800], P('tensor', 'section', 'dp'), may hold values from 0.001 to 0.1
- master_vec: float32 [16, 1300], P('dp'), may hold values from -6 to 6
- first_vec: float32 [16, 1300], P('dp'), may hold values from -4 to 4
- second_vec: float32 [16, 1300], P('dp'), may hold values from 0.001 to 0.1
Outputs:
- weights_mat: bfloat16 [4, 1600, 4800], P('tensor', 'section')
- weights_vec: bfloat16 [20800], replicated
- new_master_mat: float32 [4, 2, 16, 50, 4800], P('tensor', 'section', 'dp')
- new_first_mat: float32 [4, 2, 16, 50, 4800], P('tensor', 'section', 'dp')
- new_second_mat: float32 [4, 2, 16, 50, 4800], P('tensor', 'section', 'dp')
- new_master_vec: float32 [16, 1300], P('dp')
- new_first_vec: float32 [16, 1300], P('dp')
- new_second_vec: float32 [16, 1300], P('dp')
The draws below stay inside these ranges and needn't reach their ends.
All inputs are finite; a program needn't handle non-finite values.
Results may differ from the reference program's by a relative error of at most 0.0004.
Values may be sent and summed in bfloat16 or wider, within the bound.
No kernel may reach another device: no remote copies, remote signals or barrier semaphores. Data moves between devices by JAX's collectives and lax.ppermute only.
A program may use at most 128 MiB of HBM per device.

```python
import math
import jax
import jax.numpy as jnp
from jax import lax

D = 1600
FF = 6400
STEP = 10
COLS = 4800
OWNED_ROWS = 50
VECTOR = 20800
OWNED_VECTOR = 1300
N_DP = 16
N_TENSOR = 4
N_SECTION = 2


def draw_master_mat(key, part):
    key_base, key_rows, key_cols = jax.random.split(jax.random.fold_in(key, 11), 3)
    shape = (N_TENSOR, N_SECTION, N_DP, OWNED_ROWS, COLS)
    base = jnp.clip(jax.random.normal(key_base, shape, jnp.float32), -5.0, 5.0)
    row_scale = jnp.exp(math.log(10.0) * jax.random.uniform(key_rows, (N_TENSOR, N_SECTION, N_DP, OWNED_ROWS, 1), jnp.float32))
    col_scale = jnp.exp(math.log(3.0) * jax.random.uniform(key_cols, (1, 1, 1, 1, COLS), jnp.float32))
    owners = N_SECTION * N_DP
    owner_ramp = jnp.exp(math.log(3.0) * jnp.arange(owners, dtype=jnp.float32) / max(owners - 1, 1))
    owner_ramp = owner_ramp.reshape(1, N_SECTION, N_DP, 1, 1)
    return 0.02 * base * row_scale * col_scale * owner_ramp


def strengthened(values, key, source, target, blocks, factor):
    owner, partner = [(jnp.arange(values.shape[position]) // (values.shape[position] // blocks)).reshape([-1 if axis == position else 1 for axis in range(values.ndim)]) for position in (source, target)]
    chosen = jax.random.permutation(key, blocks)[partner]
    strong = (owner == chosen) | (owner == (partner + blocks // 2) % blocks)
    return jnp.where(strong, factor * values, values)


def level_of(key, extent, shards, low, top_value):
    level = 1.0
    for dim, parts in shards:
        heights = jax.random.uniform(jax.random.fold_in(jax.random.fold_in(key, 6), dim), (parts,), jnp.float32, low / len(shards), top_value / len(shards))
        level = level * jnp.repeat(jnp.exp(heights), extent[dim] // parts).reshape((-1,) + (1,) * (len(extent) - 1 - dim))
    return level


def centred(stream_key, shape, width, bound, cuts=(), kind=jnp.bfloat16):
    factor_of = level_of(stream_key, shape, cuts, -0.22, 0.18) if cuts else 1.0
    array = jax.random.normal(stream_key, shape, jnp.float32) * width * factor_of
    return jnp.minimum(jnp.maximum(array, -bound), bound).astype(kind)


def gaussian_with(rng, extent, width, bound, cuts, heavy, kind=jnp.bfloat16):
    entries = width * jax.random.normal(rng, extent, jnp.float32)
    if cuts:
        entries = entries * level_of(rng, extent, cuts, -0.22, 0.18)
    return jnp.clip(strengthened(entries, jax.random.fold_in(rng, 3), *heavy), -bound, bound).astype(kind)


def setup_inputs(seed: int = 0) -> dict:
    arg_keys = jax.random.split(jax.random.key(seed), 9)
    return {
        "grad_mat": gaussian_with(arg_keys[0], (N_DP, N_TENSOR, D, COLS), 1.0, 6.0, ((0, 16), (1, 4), (2, 2)), (0, 2, 16, 2.0)),
        "grad_vec": gaussian_with(arg_keys[1], (N_DP, VECTOR), 1.0, 6.0, ((0, 16),), (0, 1, 16, 2.0)),
        "master_mat": draw_master_mat(jax.random.fold_in(arg_keys[8], 71), 0),
        "first_mat": centred(arg_keys[3], (N_TENSOR, N_SECTION, N_DP, OWNED_ROWS, COLS), 0.3, 4.0, ((0, 4), (1, 2), (2, 16)), jnp.float32),
        "second_mat": jnp.clip(jnp.exp(math.log(0.1) - 4.6051702 * jax.random.uniform(arg_keys[4], (N_TENSOR, N_SECTION, N_DP, OWNED_ROWS, COLS), jnp.float32) ** level_of(arg_keys[4], (N_TENSOR, N_SECTION, N_DP, OWNED_ROWS, COLS), ((0, 4), (1, 2), (2, 16)), -0.2, 0.2)), 0.001, 0.1),
        "master_vec": centred(arg_keys[5], (N_DP, OWNED_VECTOR), 1.0, 6.0, ((0, 16),), jnp.float32),
        "first_vec": centred(arg_keys[6], (N_DP, OWNED_VECTOR), 0.3, 4.0, ((0, 16),), jnp.float32),
        "second_vec": jnp.clip(jnp.exp(math.log(0.1) - 4.6051702 * jax.random.uniform(arg_keys[7], (N_DP, OWNED_VECTOR), jnp.float32) ** level_of(arg_keys[7], (N_DP, OWNED_VECTOR), ((0, 16),), -0.2, 0.2)), 0.001, 0.1),
    }


BETA_ONE = 0.9
BETA_TWO = 0.999
EPSILON = 1e-06
LEARN_RATE = 0.25
DECAY_MAT = 0.01

def adam_direction(gradient, master, first, second, decay):
    first_new = BETA_ONE * first + (1.0 - BETA_ONE) * gradient
    second_new = BETA_TWO * second + (1.0 - BETA_TWO) * gradient * gradient
    corr_one = 1.0 - BETA_ONE ** STEP
    corr_two = 1.0 - BETA_TWO ** STEP
    direction = first_new / corr_one / (jnp.sqrt(second_new / corr_two) + EPSILON) + decay * master
    return (first_new, second_new, direction)

def segment_ratio(weight_cols, update_cols, bounds):
    pieces = []
    for index in range(len(bounds) - 1):
        lower = bounds[index]
        upper = bounds[index + 1]
        ratio = jnp.sqrt(jnp.sum(weight_cols[lower:upper])) / jnp.sqrt(jnp.sum(update_cols[lower:upper]))
        pieces.append(jnp.full((upper - lower,), ratio, dtype=weight_cols.dtype))
    return jnp.concatenate(pieces)

def reference(grad_mat, grad_vec, master_mat, first_mat, second_mat, master_vec, first_vec, second_vec):
    tensor_count = N_TENSOR
    columns = (4 * D + 2 * FF) // tensor_count
    state_shape = master_mat.shape
    gradient = lax.optimization_barrier(jnp.sum(grad_mat, axis=0, dtype=jnp.float32))
    master = master_mat.reshape(tensor_count, D, columns)
    first = first_mat.reshape(tensor_count, D, columns)
    second = second_mat.reshape(tensor_count, D, columns)
    first_new, second_new, direction = adam_direction(gradient, master, first, second, DECAY_MAT)
    bounds_mat = [0, 3 * D // tensor_count, 4 * D // tensor_count, (4 * D + FF) // tensor_count, columns]
    weight_cols = lax.optimization_barrier(jnp.sum(master * master, axis=(0, 1)))
    update_cols = lax.optimization_barrier(jnp.sum(direction * direction, axis=(0, 1)))
    ratio_cols = segment_ratio(weight_cols, update_cols, bounds_mat)
    master_new = master - LEARN_RATE * ratio_cols * direction
    length = 9 * D + FF
    vec_shape = master_vec.shape
    gradient_vec = lax.optimization_barrier(jnp.sum(grad_vec, axis=0, dtype=jnp.float32))
    master_v = master_vec.reshape(length)
    first_v, second_v, direction_v = adam_direction(gradient_vec, master_v, first_vec.reshape(length), second_vec.reshape(length), 0.0)
    bounds_vec = [0, D, 2 * D, 5 * D, 6 * D, 7 * D, 8 * D, 8 * D + FF, 9 * D + FF]
    ratio_vec = segment_ratio(master_v * master_v, direction_v * direction_v, bounds_vec)
    master_v_new = master_v - LEARN_RATE * ratio_vec * direction_v
    return (master_new.astype(jnp.bfloat16), master_v_new.astype(jnp.bfloat16), master_new.reshape(state_shape), first_new.reshape(state_shape), second_new.reshape(state_shape), master_v_new.reshape(vec_shape), first_v.reshape(vec_shape), second_v.reshape(vec_shape))
```

```python
import jax
import jax.numpy as jnp
from jax import lax
from jax.sharding import PartitionSpec as P

D = 1600
FF = 6400
STEP = 10


BETA_ONE = 0.9
BETA_TWO = 0.999
EPSILON = 1e-06
LEARN_RATE = 0.25
DECAY_MAT = 0.01


def adam_direction(gradient, master, first, second, decay):
    first_new = BETA_ONE * first + (1.0 - BETA_ONE) * gradient
    second_new = BETA_TWO * second + (1.0 - BETA_TWO) * gradient * gradient
    corr_one = 1.0 - BETA_ONE**STEP
    corr_two = 1.0 - BETA_TWO**STEP
    direction = first_new / corr_one / (jnp.sqrt(second_new / corr_two) + EPSILON) + decay * master
    return (first_new, second_new, direction)


def segment_masks(position, bounds):
    lower = jnp.array(bounds[:-1], dtype=jnp.int32)[:, None]
    upper = jnp.array(bounds[1:], dtype=jnp.int32)[:, None]
    return ((position[None, :] >= lower) & (position[None, :] < upper)).astype(jnp.float32)


def local(grad_mat, grad_vec, master_mat, first_mat, second_mat, master_vec, first_vec, second_vec):
    n_dp = lax.axis_size("dp")
    tensor_count = lax.axis_size("tensor")
    section_rows = grad_mat.shape[2]
    columns = grad_mat.shape[3]
    vec_length = grad_vec.shape[1]
    state_shape = master_mat.shape
    vec_shape = master_vec.shape
    owned_rows = state_shape[3]
    owned_vec = vec_shape[1]
    assert owned_vec <= columns and owned_rows * n_dp == section_rows
    master = master_mat.reshape(owned_rows, columns)
    master_v = master_vec.reshape(owned_vec)
    bounds_mat = [
        0,
        3 * D // tensor_count,
        4 * D // tensor_count,
        (4 * D + FF) // tensor_count,
        columns,
    ]
    masks_mat = segment_masks(lax.iota(jnp.int32, columns), bounds_mat)
    bounds_vec = [0, D, 2 * D, 5 * D, 6 * D, 7 * D, 8 * D, 8 * D + FF, 9 * D + FF]
    vec_index = lax.axis_index("dp") * owned_vec + lax.iota(jnp.int32, owned_vec)
    masks_vec = segment_masks(vec_index, bounds_vec)

    local_grad = grad_mat.reshape(n_dp, owned_rows, columns).astype(jnp.float32)
    local_vec = grad_vec.reshape(n_dp, 1, owned_vec).astype(jnp.float32)
    local_vec = jnp.pad(local_vec, ((0, 0), (0, 0), (0, columns - owned_vec)))
    payload = jnp.concatenate([local_grad, local_vec], axis=1)
    summed = lax.optimization_barrier(lax.psum_scatter(payload, "dp", scatter_dimension=0, tiled=True))
    gradient = summed[0, :owned_rows]
    gradient_v = summed[0, owned_rows, :owned_vec]

    first_new, second_new, direction = adam_direction(
        gradient, master, first_mat.reshape(owned_rows, columns), second_mat.reshape(owned_rows, columns), DECAY_MAT
    )
    first_v, second_v, direction_v = adam_direction(
        gradient_v, master_v, first_vec.reshape(owned_vec), second_vec.reshape(owned_vec), 0.0
    )
    weight_mat_sq = jnp.sum(masks_mat * jnp.sum(master * master, axis=0)[None, :], axis=1)
    weight_vec_sq = jnp.sum(masks_vec * (master_v * master_v)[None, :], axis=1)
    update_mat_sq = jnp.sum(masks_mat * jnp.sum(direction * direction, axis=0)[None, :], axis=1)
    update_vec_sq = jnp.sum(masks_vec * (direction_v * direction_v)[None, :], axis=1)

    vec_owner = (lax.axis_index("tensor") == 0) & (lax.axis_index("section") == 0)
    vec_part = jnp.where(vec_owner, jnp.concatenate([weight_vec_sq, update_vec_sq]), 0.0)
    sums = lax.psum(jnp.concatenate([weight_mat_sq, update_mat_sq, vec_part]), ("dp", "tensor", "section"))
    n_mat = weight_mat_sq.shape[0]
    n_vec = weight_vec_sq.shape[0]
    wsum_mat, usum_mat = sums[:n_mat], sums[n_mat : 2 * n_mat]
    wsum_vec, usum_vec = sums[2 * n_mat : 2 * n_mat + n_vec], sums[2 * n_mat + n_vec :]
    ratio_mat = jnp.sqrt(wsum_mat) / jnp.sqrt(usum_mat)
    ratio_vec = jnp.sqrt(wsum_vec) / jnp.sqrt(usum_vec)
    ratio_cols = jnp.sum(masks_mat * ratio_mat[:, None], axis=0)
    ratio_entries = jnp.sum(masks_vec * ratio_vec[:, None], axis=0)
    master_new = master - LEARN_RATE * ratio_cols[None, :] * direction
    master_v_new = master_v - LEARN_RATE * ratio_entries * direction_v

    weights_v_row = jnp.pad(master_v_new.astype(jnp.bfloat16), (0, columns - owned_vec))[None, :]
    weights_rows = jnp.concatenate([master_new.astype(jnp.bfloat16), weights_v_row], axis=0)
    gathered = lax.all_gather(weights_rows, "dp", axis=0, tiled=False)
    weights_mat = gathered[:, :owned_rows].reshape(1, section_rows, columns)
    weights_vec = gathered[:, owned_rows, :owned_vec].reshape(vec_length)
    return (
        weights_mat,
        weights_vec,
        master_new.reshape(state_shape),
        first_new.reshape(state_shape),
        second_new.reshape(state_shape),
        master_v_new.reshape(vec_shape),
        first_v.reshape(vec_shape),
        second_v.reshape(vec_shape),
    )


def solution(mesh):
    in_specs = (
        P("dp", "tensor", "section", None),
        P("dp", None),
        P("tensor", "section", "dp", None, None),
        P("tensor", "section", "dp", None, None),
        P("tensor", "section", "dp", None, None),
        P("dp", None),
        P("dp", None),
        P("dp", None),
    )
    out_specs = (
        P("tensor", "section", None),
        P(),
        P("tensor", "section", "dp", None, None),
        P("tensor", "section", "dp", None, None),
        P("tensor", "section", "dp", None, None),
        P("dp", None),
        P("dp", None),
        P("dp", None),
    )
    return jax.shard_map(local, mesh=mesh, in_specs=in_specs, out_specs=out_specs, check_vma=False)
```

```python
import jax
import jax.numpy as jnp
from jax import lax
from jax.sharding import PartitionSpec as P

D = 1600
FF = 6400
STEP = 10


BETA_ONE = 0.9
BETA_TWO = 0.999
EPSILON = 1e-06
LEARN_RATE = 0.25
DECAY_MAT = 0.01


def adam_direction(gradient, master, first, second, decay):
    first_new = BETA_ONE * first + (1.0 - BETA_ONE) * gradient
    second_new = BETA_TWO * second + (1.0 - BETA_TWO) * gradient * gradient
    corr_one = 1.0 - BETA_ONE**STEP
    corr_two = 1.0 - BETA_TWO**STEP
    direction = first_new / corr_one / (jnp.sqrt(second_new / corr_two) + EPSILON) + decay * master
    return (first_new, second_new, direction)


def segment_masks(position, bounds):
    lower = jnp.array(bounds[:-1], dtype=jnp.int32)[:, None]
    upper = jnp.array(bounds[1:], dtype=jnp.int32)[:, None]
    return ((position[None, :] >= lower) & (position[None, :] < upper)).astype(jnp.float32)


def butterfly_sum(x, axes):
    for axis in axes:
        size = lax.axis_size(axis)
        assert size & (size - 1) == 0
        step = 1
        while step < size:
            x = x + lax.ppermute(x, axis, [(i, i ^ step) for i in range(size)])
            step *= 2
    return x


def local(grad_mat, grad_vec, master_mat, first_mat, second_mat, master_vec, first_vec, second_vec):
    n_dp = lax.axis_size("dp")
    tensor_count = lax.axis_size("tensor")
    section_rows = grad_mat.shape[2]
    columns = grad_mat.shape[3]
    vec_length = grad_vec.shape[1]
    state_shape = master_mat.shape
    vec_shape = master_vec.shape
    owned_rows = state_shape[3]
    owned_vec = vec_shape[1]
    assert owned_vec <= columns and owned_rows * n_dp == section_rows
    master = master_mat.reshape(owned_rows, columns)
    master_v = master_vec.reshape(owned_vec)
    bounds_mat = [
        0,
        3 * D // tensor_count,
        4 * D // tensor_count,
        (4 * D + FF) // tensor_count,
        columns,
    ]
    masks_mat = segment_masks(lax.iota(jnp.int32, columns), bounds_mat)
    bounds_vec = [0, D, 2 * D, 5 * D, 6 * D, 7 * D, 8 * D, 8 * D + FF, 9 * D + FF]
    vec_index = lax.axis_index("dp") * owned_vec + lax.iota(jnp.int32, owned_vec)
    masks_vec = segment_masks(vec_index, bounds_vec)

    local_grad = grad_mat.reshape(n_dp, owned_rows, columns).astype(jnp.float32)
    local_vec = grad_vec.reshape(n_dp, 1, owned_vec).astype(jnp.float32)
    local_vec = jnp.pad(local_vec, ((0, 0), (0, 0), (0, columns - owned_vec)))
    payload = jnp.concatenate([local_grad, local_vec], axis=1)
    summed = lax.optimization_barrier(lax.psum_scatter(payload, "dp", scatter_dimension=0, tiled=True))
    gradient = summed[0, :owned_rows]
    gradient_v = summed[0, owned_rows, :owned_vec]

    first_new, second_new, direction = adam_direction(
        gradient, master, first_mat.reshape(owned_rows, columns), second_mat.reshape(owned_rows, columns), DECAY_MAT
    )
    first_v, second_v, direction_v = adam_direction(
        gradient_v, master_v, first_vec.reshape(owned_vec), second_vec.reshape(owned_vec), 0.0
    )
    weight_mat_sq = jnp.sum(masks_mat * jnp.sum(master * master, axis=0)[None, :], axis=1)
    weight_vec_sq = jnp.sum(masks_vec * (master_v * master_v)[None, :], axis=1)
    update_mat_sq = jnp.sum(masks_mat * jnp.sum(direction * direction, axis=0)[None, :], axis=1)
    update_vec_sq = jnp.sum(masks_vec * (direction_v * direction_v)[None, :], axis=1)

    vec_owner = (lax.axis_index("tensor") == 0) & (lax.axis_index("section") == 0)
    vec_part = jnp.where(vec_owner, jnp.concatenate([weight_vec_sq, update_vec_sq]), 0.0)
    sums = butterfly_sum(jnp.concatenate([weight_mat_sq, update_mat_sq, vec_part]), ("section", "tensor", "dp"))
    n_mat = weight_mat_sq.shape[0]
    n_vec = weight_vec_sq.shape[0]
    wsum_mat, usum_mat = sums[:n_mat], sums[n_mat : 2 * n_mat]
    wsum_vec, usum_vec = sums[2 * n_mat : 2 * n_mat + n_vec], sums[2 * n_mat + n_vec :]
    ratio_mat = jnp.sqrt(wsum_mat) / jnp.sqrt(usum_mat)
    ratio_vec = jnp.sqrt(wsum_vec) / jnp.sqrt(usum_vec)
    ratio_cols = jnp.sum(masks_mat * ratio_mat[:, None], axis=0)
    ratio_entries = jnp.sum(masks_vec * ratio_vec[:, None], axis=0)
    master_new = master - LEARN_RATE * ratio_cols[None, :] * direction
    master_v_new = master_v - LEARN_RATE * ratio_entries * direction_v

    weights_v_row = jnp.pad(master_v_new.astype(jnp.bfloat16), (0, columns - owned_vec))[None, :]
    weights_rows = jnp.concatenate([master_new.astype(jnp.bfloat16), weights_v_row], axis=0)
    gathered = lax.all_gather(weights_rows, "dp", axis=0, tiled=False)
    weights_mat = gathered[:, :owned_rows].reshape(1, section_rows, columns)
    weights_vec = gathered[:, owned_rows, :owned_vec].reshape(vec_length)
    return (
        weights_mat,
        weights_vec,
        master_new.reshape(state_shape),
        first_new.reshape(state_shape),
        second_new.reshape(state_shape),
        master_v_new.reshape(vec_shape),
        first_v.reshape(vec_shape),
        second_v.reshape(vec_shape),
    )


def solution(mesh):
    in_specs = (
        P("dp", "tensor", "section", None),
        P("dp", None),
        P("tensor", "section", "dp", None, None),
        P("tensor", "section", "dp", None, None),
        P("tensor", "section", "dp", None, None),
        P("dp", None),
        P("dp", None),
        P("dp", None),
    )
    out_specs = (
        P("tensor", "section", None),
        P(),
        P("tensor", "section", "dp", None, None),
        P("tensor", "section", "dp", None, None),
        P("tensor", "section", "dp", None, None),
        P("dp", None),
        P("dp", None),
        P("dp", None),
    )
    return jax.shard_map(local, mesh=mesh, in_specs=in_specs, out_specs=out_specs, check_vma=False)
```

```python
import jax
import jax.numpy as jnp
from jax import lax
from jax.sharding import PartitionSpec as P

D = 1600
FF = 6400
STEP = 10


BETA_ONE = 0.9
BETA_TWO = 0.999
EPSILON = 1e-06
LEARN_RATE = 0.25
DECAY_MAT = 0.01


def adam_direction(gradient, master, first, second, decay):
    first_new = BETA_ONE * first + (1.0 - BETA_ONE) * gradient
    second_new = BETA_TWO * second + (1.0 - BETA_TWO) * gradient * gradient
    corr_one = 1.0 - BETA_ONE**STEP
    corr_two = 1.0 - BETA_TWO**STEP
    direction = first_new / corr_one / (jnp.sqrt(second_new / corr_two) + EPSILON) + decay * master
    return (first_new, second_new, direction)


def segment_masks(position, bounds):
    lower = jnp.array(bounds[:-1], dtype=jnp.int32)[:, None]
    upper = jnp.array(bounds[1:], dtype=jnp.int32)[:, None]
    return ((position[None, :] >= lower) & (position[None, :] < upper)).astype(jnp.float32)


def butterfly_sum(x, axes):
    for axis in axes:
        size = lax.axis_size(axis)
        assert size & (size - 1) == 0
        step = 1
        while step < size:
            x = x + lax.ppermute(x, axis, [(i, i ^ step) for i in range(size)])
            step *= 2
    return x


def local(grad_mat, grad_vec, master_mat, first_mat, second_mat, master_vec, first_vec, second_vec):
    n_dp = lax.axis_size("dp")
    tensor_count = lax.axis_size("tensor")
    section_rows = grad_mat.shape[2]
    columns = grad_mat.shape[3]
    vec_length = grad_vec.shape[1]
    state_shape = master_mat.shape
    vec_shape = master_vec.shape
    owned_rows = state_shape[3]
    owned_vec = vec_shape[1]
    assert owned_vec <= columns and owned_rows * n_dp == section_rows
    master = master_mat.reshape(owned_rows, columns)
    master_v = master_vec.reshape(owned_vec)
    bounds_mat = [
        0,
        3 * D // tensor_count,
        4 * D // tensor_count,
        (4 * D + FF) // tensor_count,
        columns,
    ]
    masks_mat = segment_masks(lax.iota(jnp.int32, columns), bounds_mat)
    bounds_vec = [0, D, 2 * D, 5 * D, 6 * D, 7 * D, 8 * D, 8 * D + FF, 9 * D + FF]
    vec_index = lax.axis_index("dp") * owned_vec + lax.iota(jnp.int32, owned_vec)
    masks_vec = segment_masks(vec_index, bounds_vec)

    split = bounds_mat[3]
    assert owned_vec <= split
    grad_rows = grad_mat.reshape(n_dp, owned_rows, columns)
    local_vec = grad_vec.reshape(n_dp, 1, owned_vec).astype(jnp.float32)
    local_vec = jnp.pad(local_vec, ((0, 0), (0, 0), (0, split - owned_vec)))
    payload_a = jnp.concatenate([grad_rows[:, :, :split].astype(jnp.float32), local_vec], axis=1)
    payload_b = grad_rows[:, :, split:].astype(jnp.float32)
    summed_a = lax.optimization_barrier(lax.psum_scatter(payload_a, "dp", scatter_dimension=0, tiled=True))
    summed_b = lax.optimization_barrier(lax.psum_scatter(payload_b, "dp", scatter_dimension=0, tiled=True))
    vec_owner = (lax.axis_index("tensor") == 0) & (lax.axis_index("section") == 0)

    def matrix_chunk(gradient, lo, hi, extra):
        chunk_master = master[:, lo:hi]
        first_new, second_new, direction = adam_direction(
            gradient,
            chunk_master,
            first_mat.reshape(owned_rows, columns)[:, lo:hi],
            second_mat.reshape(owned_rows, columns)[:, lo:hi],
            DECAY_MAT,
        )
        inside = [k for k in range(len(bounds_mat) - 1) if lo <= bounds_mat[k] and bounds_mat[k + 1] <= hi]
        masks = masks_mat[inside[0] : inside[-1] + 1, lo:hi]
        weight_sq = jnp.sum(masks * jnp.sum(chunk_master * chunk_master, axis=0)[None, :], axis=1)
        update_sq = jnp.sum(masks * jnp.sum(direction * direction, axis=0)[None, :], axis=1)
        n_mat = weight_sq.shape[0]
        sums = butterfly_sum(jnp.concatenate([weight_sq, update_sq, extra]), ("section", "tensor", "dp"))
        ratio = jnp.sqrt(sums[:n_mat]) / jnp.sqrt(sums[n_mat : 2 * n_mat])
        ratio_cols = jnp.sum(masks * ratio[:, None], axis=0)
        master_new = chunk_master - LEARN_RATE * ratio_cols[None, :] * direction
        return master_new, first_new, second_new, sums[2 * n_mat :]

    gradient_v = summed_a[0, owned_rows, :owned_vec]
    first_v, second_v, direction_v = adam_direction(
        gradient_v, master_v, first_vec.reshape(owned_vec), second_vec.reshape(owned_vec), 0.0
    )
    weight_vec_sq = jnp.sum(masks_vec * (master_v * master_v)[None, :], axis=1)
    update_vec_sq = jnp.sum(masks_vec * (direction_v * direction_v)[None, :], axis=1)
    vec_part = jnp.where(vec_owner, jnp.concatenate([weight_vec_sq, update_vec_sq]), 0.0)
    master_a, first_a, second_a, vec_sums = matrix_chunk(summed_a[0, :owned_rows], 0, split, vec_part)
    n_vec = weight_vec_sq.shape[0]
    ratio_vec = jnp.sqrt(vec_sums[:n_vec]) / jnp.sqrt(vec_sums[n_vec:])
    ratio_entries = jnp.sum(masks_vec * ratio_vec[:, None], axis=0)
    master_v_new = master_v - LEARN_RATE * ratio_entries * direction_v

    weights_v_row = jnp.pad(master_v_new.astype(jnp.bfloat16), (0, split - owned_vec))[None, :]
    gathered_a = lax.all_gather(
        jnp.concatenate([master_a.astype(jnp.bfloat16), weights_v_row], axis=0), "dp", axis=0, tiled=False
    )
    master_b, first_b, second_b, _ = matrix_chunk(summed_b[0], split, columns, jnp.zeros((0,), jnp.float32))
    gathered_b = lax.all_gather(master_b.astype(jnp.bfloat16), "dp", axis=0, tiled=False)

    weights_mat = jnp.concatenate([gathered_a[:, :owned_rows], gathered_b], axis=2).reshape(1, section_rows, columns)
    weights_vec = gathered_a[:, owned_rows, :owned_vec].reshape(vec_length)
    master_new = jnp.concatenate([master_a, master_b], axis=1)
    first_new = jnp.concatenate([first_a, first_b], axis=1)
    second_new = jnp.concatenate([second_a, second_b], axis=1)
    return (
        weights_mat,
        weights_vec,
        master_new.reshape(state_shape),
        first_new.reshape(state_shape),
        second_new.reshape(state_shape),
        master_v_new.reshape(vec_shape),
        first_v.reshape(vec_shape),
        second_v.reshape(vec_shape),
    )


def solution(mesh):
    in_specs = (
        P("dp", "tensor", "section", None),
        P("dp", None),
        P("tensor", "section", "dp", None, None),
        P("tensor", "section", "dp", None, None),
        P("tensor", "section", "dp", None, None),
        P("dp", None),
        P("dp", None),
        P("dp", None),
    )
    out_specs = (
        P("tensor", "section", None),
        P(),
        P("tensor", "section", "dp", None, None),
        P("tensor", "section", "dp", None, None),
        P("tensor", "section", "dp", None, None),
        P("dp", None),
        P("dp", None),
        P("dp", None),
    )
    return jax.shard_map(local, mesh=mesh, in_specs=in_specs, out_specs=out_specs, check_vma=False)
```

```python
import jax
import jax.numpy as jnp
from jax import lax
from jax.sharding import PartitionSpec as P

D = 1600
FF = 6400
STEP = 10


BETA_ONE = 0.9
BETA_TWO = 0.999
EPSILON = 1e-06
LEARN_RATE = 0.25
DECAY_MAT = 0.01


def adam_direction(gradient, master, first, second, decay):
    first_new = BETA_ONE * first + (1.0 - BETA_ONE) * gradient
    second_new = BETA_TWO * second + (1.0 - BETA_TWO) * gradient * gradient
    corr_one = 1.0 - BETA_ONE**STEP
    corr_two = 1.0 - BETA_TWO**STEP
    direction = first_new / corr_one / (jnp.sqrt(second_new / corr_two) + EPSILON) + decay * master
    return (first_new, second_new, direction)


def segment_masks(position, bounds):
    lower = jnp.array(bounds[:-1], dtype=jnp.int32)[:, None]
    upper = jnp.array(bounds[1:], dtype=jnp.int32)[:, None]
    return ((position[None, :] >= lower) & (position[None, :] < upper)).astype(jnp.float32)


def butterfly_sum(x, axes):
    for axis in axes:
        size = lax.axis_size(axis)
        assert size & (size - 1) == 0
        step = 1
        while step < size:
            x = x + lax.ppermute(x, axis, [(i, i ^ step) for i in range(size)])
            step *= 2
    return x


def local(grad_mat, grad_vec, master_mat, first_mat, second_mat, master_vec, first_vec, second_vec):
    n_dp = lax.axis_size("dp")
    tensor_count = lax.axis_size("tensor")
    section_rows = grad_mat.shape[2]
    columns = grad_mat.shape[3]
    vec_length = grad_vec.shape[1]
    state_shape = master_mat.shape
    vec_shape = master_vec.shape
    owned_rows = state_shape[3]
    owned_vec = vec_shape[1]
    assert owned_vec <= columns and owned_rows * n_dp == section_rows
    master = master_mat.reshape(owned_rows, columns)
    master_v = master_vec.reshape(owned_vec)
    bounds_mat = [
        0,
        3 * D // tensor_count,
        4 * D // tensor_count,
        (4 * D + FF) // tensor_count,
        columns,
    ]
    masks_mat = segment_masks(lax.iota(jnp.int32, columns), bounds_mat)
    bounds_vec = [0, D, 2 * D, 5 * D, 6 * D, 7 * D, 8 * D, 8 * D + FF, 9 * D + FF]
    vec_index = lax.axis_index("dp") * owned_vec + lax.iota(jnp.int32, owned_vec)
    masks_vec = segment_masks(vec_index, bounds_vec)

    local_grad = grad_mat.reshape(n_dp, owned_rows, columns)
    local_vec = jnp.pad(grad_vec.reshape(n_dp, 1, owned_vec), ((0, 0), (0, 0), (0, columns - owned_vec)))
    payload = jnp.concatenate([local_grad, local_vec], axis=1)
    received = lax.all_to_all(payload, "dp", 0, 0, tiled=True)
    summed = jnp.sum(received.astype(jnp.float32), axis=0, keepdims=True)
    gradient = summed[0, :owned_rows]
    gradient_v = summed[0, owned_rows, :owned_vec]

    first_new, second_new, direction = adam_direction(
        gradient, master, first_mat.reshape(owned_rows, columns), second_mat.reshape(owned_rows, columns), DECAY_MAT
    )
    first_v, second_v, direction_v = adam_direction(
        gradient_v, master_v, first_vec.reshape(owned_vec), second_vec.reshape(owned_vec), 0.0
    )
    weight_mat_sq = jnp.sum(masks_mat * jnp.sum(master * master, axis=0)[None, :], axis=1)
    weight_vec_sq = jnp.sum(masks_vec * (master_v * master_v)[None, :], axis=1)
    update_mat_sq = jnp.sum(masks_mat * jnp.sum(direction * direction, axis=0)[None, :], axis=1)
    update_vec_sq = jnp.sum(masks_vec * (direction_v * direction_v)[None, :], axis=1)

    vec_owner = (lax.axis_index("tensor") == 0) & (lax.axis_index("section") == 0)
    vec_part = jnp.where(vec_owner, jnp.concatenate([weight_vec_sq, update_vec_sq]), 0.0)
    sums = butterfly_sum(jnp.concatenate([weight_mat_sq, update_mat_sq, vec_part]), ("section", "tensor", "dp"))
    n_mat = weight_mat_sq.shape[0]
    n_vec = weight_vec_sq.shape[0]
    wsum_mat, usum_mat = sums[:n_mat], sums[n_mat : 2 * n_mat]
    wsum_vec, usum_vec = sums[2 * n_mat : 2 * n_mat + n_vec], sums[2 * n_mat + n_vec :]
    ratio_mat = jnp.sqrt(wsum_mat) / jnp.sqrt(usum_mat)
    ratio_vec = jnp.sqrt(wsum_vec) / jnp.sqrt(usum_vec)
    ratio_cols = jnp.sum(masks_mat * ratio_mat[:, None], axis=0)
    ratio_entries = jnp.sum(masks_vec * ratio_vec[:, None], axis=0)
    master_new = master - LEARN_RATE * ratio_cols[None, :] * direction
    master_v_new = master_v - LEARN_RATE * ratio_entries * direction_v

    weights_v_row = jnp.pad(master_v_new.astype(jnp.bfloat16), (0, columns - owned_vec))[None, :]
    weights_rows = jnp.concatenate([master_new.astype(jnp.bfloat16), weights_v_row], axis=0)
    gathered = lax.all_gather(weights_rows, "dp", axis=0, tiled=False)
    weights_mat = gathered[:, :owned_rows].reshape(1, section_rows, columns)
    weights_vec = gathered[:, owned_rows, :owned_vec].reshape(vec_length)
    return (
        weights_mat,
        weights_vec,
        master_new.reshape(state_shape),
        first_new.reshape(state_shape),
        second_new.reshape(state_shape),
        master_v_new.reshape(vec_shape),
        first_v.reshape(vec_shape),
        second_v.reshape(vec_shape),
    )


def solution(mesh):
    in_specs = (
        P("dp", "tensor", "section", None),
        P("dp", None),
        P("tensor", "section", "dp", None, None),
        P("tensor", "section", "dp", None, None),
        P("tensor", "section", "dp", None, None),
        P("dp", None),
        P("dp", None),
        P("dp", None),
    )
    out_specs = (
        P("tensor", "section", None),
        P(),
        P("tensor", "section", "dp", None, None),
        P("tensor", "section", "dp", None, None),
        P("tensor", "section", "dp", None, None),
        P("dp", None),
        P("dp", None),
        P("dp", None),
    )
    return jax.shard_map(local, mesh=mesh, in_specs=in_specs, out_specs=out_specs, check_vma=False)
```

```python
import jax
import jax.numpy as jnp
from jax import lax
from jax.sharding import PartitionSpec as P

D = 1600
FF = 6400
STEP = 10


BETA_ONE = 0.9
BETA_TWO = 0.999
EPSILON = 1e-06
LEARN_RATE = 0.25
DECAY_MAT = 0.01


def adam_direction(gradient, master, first, second, decay):
    first_new = BETA_ONE * first + (1.0 - BETA_ONE) * gradient
    second_new = BETA_TWO * second + (1.0 - BETA_TWO) * gradient * gradient
    corr_one = 1.0 - BETA_ONE**STEP
    corr_two = 1.0 - BETA_TWO**STEP
    direction = first_new / corr_one / (jnp.sqrt(second_new / corr_two) + EPSILON) + decay * master
    return (first_new, second_new, direction)


def segment_masks(position, bounds):
    lower = jnp.array(bounds[:-1], dtype=jnp.int32)[:, None]
    upper = jnp.array(bounds[1:], dtype=jnp.int32)[:, None]
    return ((position[None, :] >= lower) & (position[None, :] < upper)).astype(jnp.float32)


def all_sum(x, axes):
    count = 1
    for axis in axes:
        count *= lax.axis_size(axis)
    copies = jnp.broadcast_to(x[None], (count,) + x.shape)
    return jnp.sum(lax.all_to_all(copies, axes, 0, 0, tiled=True), axis=0)


def local(grad_mat, grad_vec, master_mat, first_mat, second_mat, master_vec, first_vec, second_vec):
    n_dp = lax.axis_size("dp")
    tensor_count = lax.axis_size("tensor")
    section_rows = grad_mat.shape[2]
    columns = grad_mat.shape[3]
    vec_length = grad_vec.shape[1]
    state_shape = master_mat.shape
    vec_shape = master_vec.shape
    owned_rows = state_shape[3]
    owned_vec = vec_shape[1]
    assert owned_vec <= columns and owned_rows * n_dp == section_rows
    master = master_mat.reshape(owned_rows, columns)
    master_v = master_vec.reshape(owned_vec)
    bounds_mat = [
        0,
        3 * D // tensor_count,
        4 * D // tensor_count,
        (4 * D + FF) // tensor_count,
        columns,
    ]
    masks_mat = segment_masks(lax.iota(jnp.int32, columns), bounds_mat)
    bounds_vec = [0, D, 2 * D, 5 * D, 6 * D, 7 * D, 8 * D, 8 * D + FF, 9 * D + FF]
    vec_index = lax.axis_index("dp") * owned_vec + lax.iota(jnp.int32, owned_vec)
    masks_vec = segment_masks(vec_index, bounds_vec)

    local_grad = grad_mat.reshape(n_dp, owned_rows, columns).astype(jnp.float32)
    local_vec = grad_vec.reshape(n_dp, 1, owned_vec).astype(jnp.float32)
    local_vec = jnp.pad(local_vec, ((0, 0), (0, 0), (0, columns - owned_vec)))
    payload = jnp.concatenate([local_grad, local_vec], axis=1)
    summed = lax.optimization_barrier(lax.psum_scatter(payload, "dp", scatter_dimension=0, tiled=True))
    gradient = summed[0, :owned_rows]
    gradient_v = summed[0, owned_rows, :owned_vec]

    first_new, second_new, direction = adam_direction(
        gradient, master, first_mat.reshape(owned_rows, columns), second_mat.reshape(owned_rows, columns), DECAY_MAT
    )
    first_v, second_v, direction_v = adam_direction(
        gradient_v, master_v, first_vec.reshape(owned_vec), second_vec.reshape(owned_vec), 0.0
    )
    weight_mat_sq = jnp.sum(masks_mat * jnp.sum(master * master, axis=0)[None, :], axis=1)
    weight_vec_sq = jnp.sum(masks_vec * (master_v * master_v)[None, :], axis=1)
    update_mat_sq = jnp.sum(masks_mat * jnp.sum(direction * direction, axis=0)[None, :], axis=1)
    update_vec_sq = jnp.sum(masks_vec * (direction_v * direction_v)[None, :], axis=1)

    vec_owner = (lax.axis_index("tensor") == 0) & (lax.axis_index("section") == 0)
    vec_part = jnp.where(vec_owner, jnp.concatenate([weight_vec_sq, update_vec_sq]), 0.0)
    sums = all_sum(jnp.concatenate([weight_mat_sq, update_mat_sq, vec_part]), ("dp", "tensor", "section"))
    n_mat = weight_mat_sq.shape[0]
    n_vec = weight_vec_sq.shape[0]
    wsum_mat, usum_mat = sums[:n_mat], sums[n_mat : 2 * n_mat]
    wsum_vec, usum_vec = sums[2 * n_mat : 2 * n_mat + n_vec], sums[2 * n_mat + n_vec :]
    ratio_mat = jnp.sqrt(wsum_mat) / jnp.sqrt(usum_mat)
    ratio_vec = jnp.sqrt(wsum_vec) / jnp.sqrt(usum_vec)
    ratio_cols = jnp.sum(masks_mat * ratio_mat[:, None], axis=0)
    ratio_entries = jnp.sum(masks_vec * ratio_vec[:, None], axis=0)
    master_new = master - LEARN_RATE * ratio_cols[None, :] * direction
    master_v_new = master_v - LEARN_RATE * ratio_entries * direction_v

    weights_v_row = jnp.pad(master_v_new.astype(jnp.bfloat16), (0, columns - owned_vec))[None, :]
    weights_rows = jnp.concatenate([master_new.astype(jnp.bfloat16), weights_v_row], axis=0)
    gathered = lax.all_gather(weights_rows, "dp", axis=0, tiled=False)
    weights_mat = gathered[:, :owned_rows].reshape(1, section_rows, columns)
    weights_vec = gathered[:, owned_rows, :owned_vec].reshape(vec_length)
    return (
        weights_mat,
        weights_vec,
        master_new.reshape(state_shape),
        first_new.reshape(state_shape),
        second_new.reshape(state_shape),
        master_v_new.reshape(vec_shape),
        first_v.reshape(vec_shape),
        second_v.reshape(vec_shape),
    )


def solution(mesh):
    in_specs = (
        P("dp", "tensor", "section", None),
        P("dp", None),
        P("tensor", "section", "dp", None, None),
        P("tensor", "section", "dp", None, None),
        P("tensor", "section", "dp", None, None),
        P("dp", None),
        P("dp", None),
        P("dp", None),
    )
    out_specs = (
        P("tensor", "section", None),
        P(),
        P("tensor", "section", "dp", None, None),
        P("tensor", "section", "dp", None, None),
        P("tensor", "section", "dp", None, None),
        P("dp", None),
        P("dp", None),
        P("dp", None),
    )
    return jax.shard_map(local, mesh=mesh, in_specs=in_specs, out_specs=out_specs, check_vma=False)
```

```python
import jax
import jax.numpy as jnp
from jax import lax
from jax.sharding import PartitionSpec as P
from jax.experimental import pallas as pl
from jax.experimental.pallas import tpu as pltpu

D = 1600
FF = 6400
STEP = 10


BETA_ONE = 0.9
BETA_TWO = 0.999
EPSILON = 1e-06
LEARN_RATE = 0.25
DECAY_MAT = 0.01


def adam_direction(gradient, master, first, second, decay):
    first_new = BETA_ONE * first + (1.0 - BETA_ONE) * gradient
    second_new = BETA_TWO * second + (1.0 - BETA_TWO) * gradient * gradient
    corr_one = 1.0 - BETA_ONE**STEP
    corr_two = 1.0 - BETA_TWO**STEP
    direction = first_new / corr_one / (jnp.sqrt(second_new / corr_two) + EPSILON) + decay * master
    return (first_new, second_new, direction)


def segment_masks(position, bounds):
    lower = jnp.array(bounds[:-1], dtype=jnp.int32)[:, None]
    upper = jnp.array(bounds[1:], dtype=jnp.int32)[:, None]
    return ((position[None, :] >= lower) & (position[None, :] < upper)).astype(jnp.float32)


def all_sum(x, axes):
    count = 1
    for axis in axes:
        count *= lax.axis_size(axis)
    copies = jnp.broadcast_to(x[None], (count,) + x.shape)
    return jnp.sum(lax.all_to_all(copies, axes, 0, 0, tiled=True), axis=0)


def regroup_kernel(owned_rows, rows_ref, vec_ref, out_ref):
    for j in range(out_ref.shape[0]):
        out_ref[j, :owned_rows, :] = rows_ref[j * owned_rows : (j + 1) * owned_rows, :].astype(jnp.float32)
        out_ref[j, owned_rows:, :] = vec_ref[j : j + 1, :]


def regroup(rows, vec_rows, n_owners, owned_rows):
    columns = rows.shape[1]
    per_step = 8
    assert n_owners % per_step == 0
    return pl.pallas_call(
        lambda r, v, o: regroup_kernel(owned_rows, r, v, o),
        grid=(n_owners // per_step,),
        in_specs=[
            pl.BlockSpec((per_step * owned_rows, columns), lambda i: (i, 0)),
            pl.BlockSpec((per_step, columns), lambda i: (i, 0)),
        ],
        out_specs=pl.BlockSpec((per_step, owned_rows + 1, columns), lambda i: (i, 0, 0)),
        out_shape=jax.ShapeDtypeStruct((n_owners, owned_rows + 1, columns), jnp.float32),
        compiler_params=pltpu.CompilerParams(vmem_limit_bytes=48 * 1024 * 1024),
    )(rows, vec_rows)


def local(grad_mat, grad_vec, master_mat, first_mat, second_mat, master_vec, first_vec, second_vec):
    n_dp = lax.axis_size("dp")
    tensor_count = lax.axis_size("tensor")
    section_rows = grad_mat.shape[2]
    columns = grad_mat.shape[3]
    vec_length = grad_vec.shape[1]
    state_shape = master_mat.shape
    vec_shape = master_vec.shape
    owned_rows = state_shape[3]
    owned_vec = vec_shape[1]
    assert owned_vec <= columns and owned_rows * n_dp == section_rows
    master = master_mat.reshape(owned_rows, columns)
    master_v = master_vec.reshape(owned_vec)
    bounds_mat = [
        0,
        3 * D // tensor_count,
        4 * D // tensor_count,
        (4 * D + FF) // tensor_count,
        columns,
    ]
    masks_mat = segment_masks(lax.iota(jnp.int32, columns), bounds_mat)
    bounds_vec = [0, D, 2 * D, 5 * D, 6 * D, 7 * D, 8 * D, 8 * D + FF, 9 * D + FF]
    vec_index = lax.axis_index("dp") * owned_vec + lax.iota(jnp.int32, owned_vec)
    masks_vec = segment_masks(vec_index, bounds_vec)

    local_vec = jnp.pad(grad_vec.reshape(n_dp, owned_vec).astype(jnp.float32), ((0, 0), (0, columns - owned_vec)))
    payload = regroup(grad_mat.reshape(section_rows, columns), local_vec, n_dp, owned_rows)
    summed = lax.optimization_barrier(lax.psum_scatter(payload, "dp", scatter_dimension=0, tiled=True))
    gradient = summed[0, :owned_rows]
    gradient_v = summed[0, owned_rows, :owned_vec]

    first_new, second_new, direction = adam_direction(
        gradient, master, first_mat.reshape(owned_rows, columns), second_mat.reshape(owned_rows, columns), DECAY_MAT
    )
    first_v, second_v, direction_v = adam_direction(
        gradient_v, master_v, first_vec.reshape(owned_vec), second_vec.reshape(owned_vec), 0.0
    )
    weight_mat_sq = jnp.sum(masks_mat * jnp.sum(master * master, axis=0)[None, :], axis=1)
    weight_vec_sq = jnp.sum(masks_vec * (master_v * master_v)[None, :], axis=1)
    update_mat_sq = jnp.sum(masks_mat * jnp.sum(direction * direction, axis=0)[None, :], axis=1)
    update_vec_sq = jnp.sum(masks_vec * (direction_v * direction_v)[None, :], axis=1)

    vec_owner = (lax.axis_index("tensor") == 0) & (lax.axis_index("section") == 0)
    vec_part = jnp.where(vec_owner, jnp.concatenate([weight_vec_sq, update_vec_sq]), 0.0)
    sums = all_sum(jnp.concatenate([weight_mat_sq, update_mat_sq, vec_part]), ("dp", "tensor", "section"))
    n_mat = weight_mat_sq.shape[0]
    n_vec = weight_vec_sq.shape[0]
    wsum_mat, usum_mat = sums[:n_mat], sums[n_mat : 2 * n_mat]
    wsum_vec, usum_vec = sums[2 * n_mat : 2 * n_mat + n_vec], sums[2 * n_mat + n_vec :]
    ratio_mat = jnp.sqrt(wsum_mat) / jnp.sqrt(usum_mat)
    ratio_vec = jnp.sqrt(wsum_vec) / jnp.sqrt(usum_vec)
    ratio_cols = jnp.sum(masks_mat * ratio_mat[:, None], axis=0)
    ratio_entries = jnp.sum(masks_vec * ratio_vec[:, None], axis=0)
    master_new = master - LEARN_RATE * ratio_cols[None, :] * direction
    master_v_new = master_v - LEARN_RATE * ratio_entries * direction_v

    weights_v_row = jnp.pad(master_v_new.astype(jnp.bfloat16), (0, columns - owned_vec))[None, :]
    weights_rows = jnp.concatenate([master_new.astype(jnp.bfloat16), weights_v_row], axis=0)
    gathered = lax.all_gather(weights_rows, "dp", axis=0, tiled=False)
    weights_mat = gathered[:, :owned_rows].reshape(1, section_rows, columns)
    weights_vec = gathered[:, owned_rows, :owned_vec].reshape(vec_length)
    return (
        weights_mat,
        weights_vec,
        master_new.reshape(state_shape),
        first_new.reshape(state_shape),
        second_new.reshape(state_shape),
        master_v_new.reshape(vec_shape),
        first_v.reshape(vec_shape),
        second_v.reshape(vec_shape),
    )


def solution(mesh):
    in_specs = (
        P("dp", "tensor", "section", None),
        P("dp", None),
        P("tensor", "section", "dp", None, None),
        P("tensor", "section", "dp", None, None),
        P("tensor", "section", "dp", None, None),
        P("dp", None),
        P("dp", None),
        P("dp", None),
    )
    out_specs = (
        P("tensor", "section", None),
        P(),
        P("tensor", "section", "dp", None, None),
        P("tensor", "section", "dp", None, None),
        P("tensor", "section", "dp", None, None),
        P("dp", None),
        P("dp", None),
        P("dp", None),
    )
    return jax.shard_map(local, mesh=mesh, in_specs=in_specs, out_specs=out_specs, check_vma=False)
```

```python
import jax
import jax.numpy as jnp
from jax import lax
from jax.sharding import PartitionSpec as P
from jax.experimental import pallas as pl
from jax.experimental.pallas import tpu as pltpu

D = 1600
FF = 6400
STEP = 10


BETA_ONE = 0.9
BETA_TWO = 0.999
EPSILON = 1e-06
LEARN_RATE = 0.25
DECAY_MAT = 0.01


def adam_direction(gradient, master, first, second, decay):
    first_new = BETA_ONE * first + (1.0 - BETA_ONE) * gradient
    second_new = BETA_TWO * second + (1.0 - BETA_TWO) * gradient * gradient
    corr_one = 1.0 - BETA_ONE**STEP
    corr_two = 1.0 - BETA_TWO**STEP
    direction = first_new / corr_one / (jnp.sqrt(second_new / corr_two) + EPSILON) + decay * master
    return (first_new, second_new, direction)


def segment_masks(position, bounds):
    lower = jnp.array(bounds[:-1], dtype=jnp.int32)[:, None]
    upper = jnp.array(bounds[1:], dtype=jnp.int32)[:, None]
    return ((position[None, :] >= lower) & (position[None, :] < upper)).astype(jnp.float32)


def all_sum(x, axes):
    count = 1
    for axis in axes:
        count *= lax.axis_size(axis)
    copies = jnp.broadcast_to(x[None], (count,) + x.shape)
    return jnp.sum(lax.all_to_all(copies, axes, 0, 0, tiled=True), axis=0)


def regroup_kernel(owned_rows, rows_ref, vec_ref, out_ref):
    for j in range(out_ref.shape[0]):
        out_ref[j, :owned_rows, :] = rows_ref[j * owned_rows : (j + 1) * owned_rows, :].astype(jnp.float32)
        out_ref[j, owned_rows:, :] = vec_ref[j : j + 1, :]


def regroup(rows, vec_rows, n_owners, owned_rows):
    columns = rows.shape[1]
    per_step = 8
    assert n_owners % per_step == 0
    return pl.pallas_call(
        lambda r, v, o: regroup_kernel(owned_rows, r, v, o),
        grid=(n_owners // per_step,),
        in_specs=[
            pl.BlockSpec((per_step * owned_rows, columns), lambda i: (i, 0)),
            pl.BlockSpec((per_step, columns), lambda i: (i, 0)),
        ],
        out_specs=pl.BlockSpec((per_step, owned_rows + 1, columns), lambda i: (i, 0, 0)),
        out_shape=jax.ShapeDtypeStruct((n_owners, owned_rows + 1, columns), jnp.float32),
        compiler_params=pltpu.CompilerParams(vmem_limit_bytes=48 * 1024 * 1024),
    )(rows, vec_rows)


def ungroup_kernel(owned_rows, in_ref, out_ref):
    for j in range(in_ref.shape[0]):
        out_ref[j * owned_rows : (j + 1) * owned_rows, :] = in_ref[j, :owned_rows, :]


def ungroup(gathered, owned_rows):
    n_owners, _, columns = gathered.shape
    per_step = 8
    assert n_owners % per_step == 0
    return pl.pallas_call(
        lambda i, o: ungroup_kernel(owned_rows, i, o),
        grid=(n_owners // per_step,),
        in_specs=[pl.BlockSpec((per_step, gathered.shape[1], columns), lambda i: (i, 0, 0))],
        out_specs=pl.BlockSpec((per_step * owned_rows, columns), lambda i: (i, 0)),
        out_shape=jax.ShapeDtypeStruct((n_owners * owned_rows, columns), gathered.dtype),
        compiler_params=pltpu.CompilerParams(vmem_limit_bytes=48 * 1024 * 1024),
    )(gathered)


def local(grad_mat, grad_vec, master_mat, first_mat, second_mat, master_vec, first_vec, second_vec):
    n_dp = lax.axis_size("dp")
    tensor_count = lax.axis_size("tensor")
    section_rows = grad_mat.shape[2]
    columns = grad_mat.shape[3]
    vec_length = grad_vec.shape[1]
    state_shape = master_mat.shape
    vec_shape = master_vec.shape
    owned_rows = state_shape[3]
    owned_vec = vec_shape[1]
    assert owned_vec <= columns and owned_rows * n_dp == section_rows
    master = master_mat.reshape(owned_rows, columns)
    master_v = master_vec.reshape(owned_vec)
    bounds_mat = [
        0,
        3 * D // tensor_count,
        4 * D // tensor_count,
        (4 * D + FF) // tensor_count,
        columns,
    ]
    masks_mat = segment_masks(lax.iota(jnp.int32, columns), bounds_mat)
    bounds_vec = [0, D, 2 * D, 5 * D, 6 * D, 7 * D, 8 * D, 8 * D + FF, 9 * D + FF]
    vec_index = lax.axis_index("dp") * owned_vec + lax.iota(jnp.int32, owned_vec)
    masks_vec = segment_masks(vec_index, bounds_vec)

    local_vec = jnp.pad(grad_vec.reshape(n_dp, owned_vec).astype(jnp.float32), ((0, 0), (0, columns - owned_vec)))
    payload = regroup(grad_mat.reshape(section_rows, columns), local_vec, n_dp, owned_rows)
    summed = lax.optimization_barrier(lax.psum_scatter(payload, "dp", scatter_dimension=0, tiled=True))
    gradient = summed[0, :owned_rows]
    gradient_v = summed[0, owned_rows, :owned_vec]

    first_new, second_new, direction = adam_direction(
        gradient, master, first_mat.reshape(owned_rows, columns), second_mat.reshape(owned_rows, columns), DECAY_MAT
    )
    first_v, second_v, direction_v = adam_direction(
        gradient_v, master_v, first_vec.reshape(owned_vec), second_vec.reshape(owned_vec), 0.0
    )
    weight_mat_sq = jnp.sum(masks_mat * jnp.sum(master * master, axis=0)[None, :], axis=1)
    weight_vec_sq = jnp.sum(masks_vec * (master_v * master_v)[None, :], axis=1)
    update_mat_sq = jnp.sum(masks_mat * jnp.sum(direction * direction, axis=0)[None, :], axis=1)
    update_vec_sq = jnp.sum(masks_vec * (direction_v * direction_v)[None, :], axis=1)

    vec_owner = (lax.axis_index("tensor") == 0) & (lax.axis_index("section") == 0)
    vec_part = jnp.where(vec_owner, jnp.concatenate([weight_vec_sq, update_vec_sq]), 0.0)
    sums = all_sum(jnp.concatenate([weight_mat_sq, update_mat_sq, vec_part]), ("dp", "tensor", "section"))
    n_mat = weight_mat_sq.shape[0]
    n_vec = weight_vec_sq.shape[0]
    wsum_mat, usum_mat = sums[:n_mat], sums[n_mat : 2 * n_mat]
    wsum_vec, usum_vec = sums[2 * n_mat : 2 * n_mat + n_vec], sums[2 * n_mat + n_vec :]
    ratio_mat = jnp.sqrt(wsum_mat) / jnp.sqrt(usum_mat)
    ratio_vec = jnp.sqrt(wsum_vec) / jnp.sqrt(usum_vec)
    ratio_cols = jnp.sum(masks_mat * ratio_mat[:, None], axis=0)
    ratio_entries = jnp.sum(masks_vec * ratio_vec[:, None], axis=0)
    master_new = master - LEARN_RATE * ratio_cols[None, :] * direction
    master_v_new = master_v - LEARN_RATE * ratio_entries * direction_v

    weights_v_row = jnp.pad(master_v_new.astype(jnp.bfloat16), (0, columns - owned_vec))[None, :]
    weights_rows = jnp.concatenate([master_new.astype(jnp.bfloat16), weights_v_row], axis=0)
    gathered = lax.all_gather(weights_rows, "dp", axis=0, tiled=False)
    weights_mat = ungroup(gathered, owned_rows).reshape(1, section_rows, columns)
    weights_vec = gathered[:, owned_rows, :owned_vec].reshape(vec_length)
    return (
        weights_mat,
        weights_vec,
        master_new.reshape(state_shape),
        first_new.reshape(state_shape),
        second_new.reshape(state_shape),
        master_v_new.reshape(vec_shape),
        first_v.reshape(vec_shape),
        second_v.reshape(vec_shape),
    )


def solution(mesh):
    in_specs = (
        P("dp", "tensor", "section", None),
        P("dp", None),
        P("tensor", "section", "dp", None, None),
        P("tensor", "section", "dp", None, None),
        P("tensor", "section", "dp", None, None),
        P("dp", None),
        P("dp", None),
        P("dp", None),
    )
    out_specs = (
        P("tensor", "section", None),
        P(),
        P("tensor", "section", "dp", None, None),
        P("tensor", "section", "dp", None, None),
        P("tensor", "section", "dp", None, None),
        P("dp", None),
        P("dp", None),
        P("dp", None),
    )
    return jax.shard_map(local, mesh=mesh, in_specs=in_specs, out_specs=out_specs, check_vma=False)
```

```python
import jax
import jax.numpy as jnp
from jax import lax
from jax.sharding import PartitionSpec as P
from jax.experimental import pallas as pl
from jax.experimental.pallas import tpu as pltpu

D = 1600
FF = 6400
STEP = 10


BETA_ONE = 0.9
BETA_TWO = 0.999
EPSILON = 1e-06
LEARN_RATE = 0.25
DECAY_MAT = 0.01


def adam_direction(gradient, master, first, second, decay):
    first_new = BETA_ONE * first + (1.0 - BETA_ONE) * gradient
    second_new = BETA_TWO * second + (1.0 - BETA_TWO) * gradient * gradient
    corr_one = 1.0 - BETA_ONE**STEP
    corr_two = 1.0 - BETA_TWO**STEP
    direction = first_new / corr_one / (jnp.sqrt(second_new / corr_two) + EPSILON) + decay * master
    return (first_new, second_new, direction)


def segment_masks(position, bounds):
    lower = jnp.array(bounds[:-1], dtype=jnp.int32)[:, None]
    upper = jnp.array(bounds[1:], dtype=jnp.int32)[:, None]
    return ((position[None, :] >= lower) & (position[None, :] < upper)).astype(jnp.float32)


def all_sum(x, axes):
    count = 1
    for axis in axes:
        count *= lax.axis_size(axis)
    copies = jnp.broadcast_to(x[None], (count,) + x.shape)
    return jnp.sum(lax.all_to_all(copies, axes, 0, 0, tiled=True), axis=0)


def regroup_kernel(owned_rows, rows_ref, vec_ref, out_ref):
    for j in range(out_ref.shape[0]):
        out_ref[j, :owned_rows, :] = rows_ref[j * owned_rows : (j + 1) * owned_rows, :].astype(jnp.float32)
        out_ref[j, owned_rows:, :] = vec_ref[j]


def regroup(rows, vec_rows, n_owners, owned_rows):
    columns = rows.shape[1]
    per_step = 4
    assert n_owners % per_step == 0
    return pl.pallas_call(
        lambda r, v, o: regroup_kernel(owned_rows, r, v, o),
        grid=(n_owners // per_step,),
        in_specs=[
            pl.BlockSpec((per_step * owned_rows, columns), lambda i: (i, 0)),
            pl.BlockSpec((per_step, 1, columns), lambda i: (i, 0, 0)),
        ],
        out_specs=pl.BlockSpec((per_step, owned_rows + 1, columns), lambda i: (i, 0, 0)),
        out_shape=jax.ShapeDtypeStruct((n_owners, owned_rows + 1, columns), jnp.float32),
        compiler_params=pltpu.CompilerParams(vmem_limit_bytes=48 * 1024 * 1024),
    )(rows, vec_rows.reshape(n_owners, 1, columns))


def ungroup_kernel(owned_rows, in_ref, out_ref):
    for j in range(in_ref.shape[0]):
        out_ref[j * owned_rows : (j + 1) * owned_rows, :] = in_ref[j, :owned_rows, :]


def ungroup(gathered, owned_rows):
    n_owners, _, columns = gathered.shape
    per_step = 4
    assert n_owners % per_step == 0
    return pl.pallas_call(
        lambda i, o: ungroup_kernel(owned_rows, i, o),
        grid=(n_owners // per_step,),
        in_specs=[pl.BlockSpec((per_step, gathered.shape[1], columns), lambda i: (i, 0, 0))],
        out_specs=pl.BlockSpec((per_step * owned_rows, columns), lambda i: (i, 0)),
        out_shape=jax.ShapeDtypeStruct((n_owners * owned_rows, columns), gathered.dtype),
        compiler_params=pltpu.CompilerParams(vmem_limit_bytes=48 * 1024 * 1024),
    )(gathered)


def local(grad_mat, grad_vec, master_mat, first_mat, second_mat, master_vec, first_vec, second_vec):
    n_dp = lax.axis_size("dp")
    tensor_count = lax.axis_size("tensor")
    section_rows = grad_mat.shape[2]
    columns = grad_mat.shape[3]
    vec_length = grad_vec.shape[1]
    state_shape = master_mat.shape
    vec_shape = master_vec.shape
    owned_rows = state_shape[3]
    owned_vec = vec_shape[1]
    assert owned_vec <= columns and owned_rows * n_dp == section_rows
    master = master_mat.reshape(owned_rows, columns)
    master_v = master_vec.reshape(owned_vec)
    bounds_mat = [
        0,
        3 * D // tensor_count,
        4 * D // tensor_count,
        (4 * D + FF) // tensor_count,
        columns,
    ]
    masks_mat = segment_masks(lax.iota(jnp.int32, columns), bounds_mat)
    bounds_vec = [0, D, 2 * D, 5 * D, 6 * D, 7 * D, 8 * D, 8 * D + FF, 9 * D + FF]
    vec_index = lax.axis_index("dp") * owned_vec + lax.iota(jnp.int32, owned_vec)
    masks_vec = segment_masks(vec_index, bounds_vec)

    local_vec = jnp.pad(grad_vec.reshape(n_dp, owned_vec).astype(jnp.float32), ((0, 0), (0, columns - owned_vec)))
    payload = regroup(grad_mat.reshape(section_rows, columns), local_vec, n_dp, owned_rows)
    summed = lax.optimization_barrier(lax.psum_scatter(payload, "dp", scatter_dimension=0, tiled=True))
    gradient = summed[0, :owned_rows]
    gradient_v = summed[0, owned_rows, :owned_vec]

    first_new, second_new, direction = adam_direction(
        gradient, master, first_mat.reshape(owned_rows, columns), second_mat.reshape(owned_rows, columns), DECAY_MAT
    )
    first_v, second_v, direction_v = adam_direction(
        gradient_v, master_v, first_vec.reshape(owned_vec), second_vec.reshape(owned_vec), 0.0
    )
    weight_mat_sq = jnp.sum(masks_mat * jnp.sum(master * master, axis=0)[None, :], axis=1)
    weight_vec_sq = jnp.sum(masks_vec * (master_v * master_v)[None, :], axis=1)
    update_mat_sq = jnp.sum(masks_mat * jnp.sum(direction * direction, axis=0)[None, :], axis=1)
    update_vec_sq = jnp.sum(masks_vec * (direction_v * direction_v)[None, :], axis=1)

    vec_owner = (lax.axis_index("tensor") == 0) & (lax.axis_index("section") == 0)
    vec_part = jnp.where(vec_owner, jnp.concatenate([weight_vec_sq, update_vec_sq]), 0.0)
    sums = all_sum(jnp.concatenate([weight_mat_sq, update_mat_sq, vec_part]), ("dp", "tensor", "section"))
    n_mat = weight_mat_sq.shape[0]
    n_vec = weight_vec_sq.shape[0]
    wsum_mat, usum_mat = sums[:n_mat], sums[n_mat : 2 * n_mat]
    wsum_vec, usum_vec = sums[2 * n_mat : 2 * n_mat + n_vec], sums[2 * n_mat + n_vec :]
    ratio_mat = jnp.sqrt(wsum_mat) / jnp.sqrt(usum_mat)
    ratio_vec = jnp.sqrt(wsum_vec) / jnp.sqrt(usum_vec)
    ratio_cols = jnp.sum(masks_mat * ratio_mat[:, None], axis=0)
    ratio_entries = jnp.sum(masks_vec * ratio_vec[:, None], axis=0)
    master_new = master - LEARN_RATE * ratio_cols[None, :] * direction
    master_v_new = master_v - LEARN_RATE * ratio_entries * direction_v

    weights_v_row = jnp.pad(master_v_new.astype(jnp.bfloat16), (0, columns - owned_vec))[None, :]
    weights_rows = jnp.concatenate([master_new.astype(jnp.bfloat16), weights_v_row], axis=0)
    gathered = lax.all_gather(weights_rows, "dp", axis=0, tiled=False)
    weights_mat = ungroup(gathered, owned_rows).reshape(1, section_rows, columns)
    weights_vec = gathered[:, owned_rows, :owned_vec].reshape(vec_length)
    return (
        weights_mat,
        weights_vec,
        master_new.reshape(state_shape),
        first_new.reshape(state_shape),
        second_new.reshape(state_shape),
        master_v_new.reshape(vec_shape),
        first_v.reshape(vec_shape),
        second_v.reshape(vec_shape),
    )


def solution(mesh):
    in_specs = (
        P("dp", "tensor", "section", None),
        P("dp", None),
        P("tensor", "section", "dp", None, None),
        P("tensor", "section", "dp", None, None),
        P("tensor", "section", "dp", None, None),
        P("dp", None),
        P("dp", None),
        P("dp", None),
    )
    out_specs = (
        P("tensor", "section", None),
        P(),
        P("tensor", "section", "dp", None, None),
        P("tensor", "section", "dp", None, None),
        P("tensor", "section", "dp", None, None),
        P("dp", None),
        P("dp", None),
        P("dp", None),
    )
    return jax.shard_map(local, mesh=mesh, in_specs=in_specs, out_specs=out_specs, check_vma=False)
```

```python
import jax
import jax.numpy as jnp
from jax import lax
from jax.sharding import PartitionSpec as P
from jax.experimental import pallas as pl
from jax.experimental.pallas import tpu as pltpu

D = 1600
FF = 6400
STEP = 10


BETA_ONE = 0.9
BETA_TWO = 0.999
EPSILON = 1e-06
LEARN_RATE = 0.25
DECAY_MAT = 0.01


def adam_direction(gradient, master, first, second, decay):
    first_new = BETA_ONE * first + (1.0 - BETA_ONE) * gradient
    second_new = BETA_TWO * second + (1.0 - BETA_TWO) * gradient * gradient
    corr_one = 1.0 - BETA_ONE**STEP
    corr_two = 1.0 - BETA_TWO**STEP
    direction = first_new / corr_one / (jnp.sqrt(second_new / corr_two) + EPSILON) + decay * master
    return (first_new, second_new, direction)


def segment_masks(position, bounds):
    lower = jnp.array(bounds[:-1], dtype=jnp.int32)[:, None]
    upper = jnp.array(bounds[1:], dtype=jnp.int32)[:, None]
    return ((position[None, :] >= lower) & (position[None, :] < upper)).astype(jnp.float32)


def all_sum(x, axes):
    count = 1
    for axis in axes:
        count *= lax.axis_size(axis)
    copies = jnp.broadcast_to(x[None], (count,) + x.shape)
    return jnp.sum(lax.all_to_all(copies, axes, 0, 0, tiled=True), axis=0)


def regroup_kernel(owned_rows, rows_ref, vec_ref, out_ref):
    for j in range(out_ref.shape[0]):
        out_ref[j, :owned_rows, :] = rows_ref[j * owned_rows : (j + 1) * owned_rows, :].astype(jnp.float32)
        out_ref[j, owned_rows:, :] = vec_ref[j : j + 1, :]


def regroup(rows, vec_rows, n_owners, owned_rows):
    columns = rows.shape[1]
    per_step = 8
    assert n_owners % per_step == 0
    return pl.pallas_call(
        lambda r, v, o: regroup_kernel(owned_rows, r, v, o),
        grid=(n_owners // per_step,),
        in_specs=[
            pl.BlockSpec((per_step * owned_rows, columns), lambda i: (i, 0)),
            pl.BlockSpec((per_step, columns), lambda i: (i, 0)),
        ],
        out_specs=pl.BlockSpec((per_step, owned_rows + 1, columns), lambda i: (i, 0, 0)),
        out_shape=jax.ShapeDtypeStruct((n_owners, owned_rows + 1, columns), jnp.float32),
        compiler_params=pltpu.CompilerParams(vmem_limit_bytes=48 * 1024 * 1024),
    )(rows, vec_rows)


def ungroup_kernel(owned_rows, in_ref, out_ref, vec_ref):
    owned_vec = vec_ref.shape[2]
    for j in range(in_ref.shape[0]):
        out_ref[j * owned_rows : (j + 1) * owned_rows, :] = in_ref[j, :owned_rows, :]
        vec_ref[j] = in_ref[j, owned_rows:, :owned_vec]


def ungroup(gathered, owned_rows, owned_vec):
    n_owners, _, columns = gathered.shape
    per_step = 8
    assert n_owners % per_step == 0
    return pl.pallas_call(
        lambda i, o, v: ungroup_kernel(owned_rows, i, o, v),
        grid=(n_owners // per_step,),
        in_specs=[pl.BlockSpec((per_step, gathered.shape[1], columns), lambda i: (i, 0, 0))],
        out_specs=[
            pl.BlockSpec((per_step * owned_rows, columns), lambda i: (i, 0)),
            pl.BlockSpec((per_step, 1, owned_vec), lambda i: (i, 0, 0)),
        ],
        out_shape=[
            jax.ShapeDtypeStruct((n_owners * owned_rows, columns), gathered.dtype),
            jax.ShapeDtypeStruct((n_owners, 1, owned_vec), gathered.dtype),
        ],
        compiler_params=pltpu.CompilerParams(vmem_limit_bytes=48 * 1024 * 1024),
    )(gathered)


def local(grad_mat, grad_vec, master_mat, first_mat, second_mat, master_vec, first_vec, second_vec):
    n_dp = lax.axis_size("dp")
    tensor_count = lax.axis_size("tensor")
    section_rows = grad_mat.shape[2]
    columns = grad_mat.shape[3]
    vec_length = grad_vec.shape[1]
    state_shape = master_mat.shape
    vec_shape = master_vec.shape
    owned_rows = state_shape[3]
    owned_vec = vec_shape[1]
    assert owned_vec <= columns and owned_rows * n_dp == section_rows
    master = master_mat.reshape(owned_rows, columns)
    master_v = master_vec.reshape(owned_vec)
    bounds_mat = [
        0,
        3 * D // tensor_count,
        4 * D // tensor_count,
        (4 * D + FF) // tensor_count,
        columns,
    ]
    masks_mat = segment_masks(lax.iota(jnp.int32, columns), bounds_mat)
    bounds_vec = [0, D, 2 * D, 5 * D, 6 * D, 7 * D, 8 * D, 8 * D + FF, 9 * D + FF]
    vec_index = lax.axis_index("dp") * owned_vec + lax.iota(jnp.int32, owned_vec)
    masks_vec = segment_masks(vec_index, bounds_vec)

    local_vec = jnp.pad(grad_vec.reshape(n_dp, owned_vec).astype(jnp.float32), ((0, 0), (0, columns - owned_vec)))
    payload = regroup(grad_mat.reshape(section_rows, columns), local_vec, n_dp, owned_rows)
    summed = lax.optimization_barrier(lax.psum_scatter(payload, "dp", scatter_dimension=0, tiled=True))
    gradient = summed[0, :owned_rows]
    gradient_v = summed[0, owned_rows, :owned_vec]

    first_new, second_new, direction = adam_direction(
        gradient, master, first_mat.reshape(owned_rows, columns), second_mat.reshape(owned_rows, columns), DECAY_MAT
    )
    first_v, second_v, direction_v = adam_direction(
        gradient_v, master_v, first_vec.reshape(owned_vec), second_vec.reshape(owned_vec), 0.0
    )
    weight_mat_sq = jnp.sum(masks_mat * jnp.sum(master * master, axis=0)[None, :], axis=1)
    weight_vec_sq = jnp.sum(masks_vec * (master_v * master_v)[None, :], axis=1)
    update_mat_sq = jnp.sum(masks_mat * jnp.sum(direction * direction, axis=0)[None, :], axis=1)
    update_vec_sq = jnp.sum(masks_vec * (direction_v * direction_v)[None, :], axis=1)

    vec_owner = (lax.axis_index("tensor") == 0) & (lax.axis_index("section") == 0)
    vec_part = jnp.where(vec_owner, jnp.concatenate([weight_vec_sq, update_vec_sq]), 0.0)
    sums = all_sum(jnp.concatenate([weight_mat_sq, update_mat_sq, vec_part]), ("dp", "tensor", "section"))
    n_mat = weight_mat_sq.shape[0]
    n_vec = weight_vec_sq.shape[0]
    wsum_mat, usum_mat = sums[:n_mat], sums[n_mat : 2 * n_mat]
    wsum_vec, usum_vec = sums[2 * n_mat : 2 * n_mat + n_vec], sums[2 * n_mat + n_vec :]
    ratio_mat = jnp.sqrt(wsum_mat) / jnp.sqrt(usum_mat)
    ratio_vec = jnp.sqrt(wsum_vec) / jnp.sqrt(usum_vec)
    ratio_cols = jnp.sum(masks_mat * ratio_mat[:, None], axis=0)
    ratio_entries = jnp.sum(masks_vec * ratio_vec[:, None], axis=0)
    master_new = master - LEARN_RATE * ratio_cols[None, :] * direction
    master_v_new = master_v - LEARN_RATE * ratio_entries * direction_v

    weights_v_row = jnp.pad(master_v_new.astype(jnp.bfloat16), (0, columns - owned_vec))[None, :]
    weights_rows = jnp.concatenate([master_new.astype(jnp.bfloat16), weights_v_row], axis=0)
    gathered = lax.all_gather(weights_rows, "dp", axis=0, tiled=False)
    weights_rows, weights_v_rows = ungroup(gathered, owned_rows, owned_vec)
    weights_mat = weights_rows.reshape(1, section_rows, columns)
    weights_vec = weights_v_rows.reshape(vec_length)
    return (
        weights_mat,
        weights_vec,
        master_new.reshape(state_shape),
        first_new.reshape(state_shape),
        second_new.reshape(state_shape),
        master_v_new.reshape(vec_shape),
        first_v.reshape(vec_shape),
        second_v.reshape(vec_shape),
    )


def solution(mesh):
    in_specs = (
        P("dp", "tensor", "section", None),
        P("dp", None),
        P("tensor", "section", "dp", None, None),
        P("tensor", "section", "dp", None, None),
        P("tensor", "section", "dp", None, None),
        P("dp", None),
        P("dp", None),
        P("dp", None),
    )
    out_specs = (
        P("tensor", "section", None),
        P(),
        P("tensor", "section", "dp", None, None),
        P("tensor", "section", "dp", None, None),
        P("tensor", "section", "dp", None, None),
        P("dp", None),
        P("dp", None),
        P("dp", None),
    )
    return jax.shard_map(local, mesh=mesh, in_specs=in_specs, out_specs=out_specs, check_vma=False)
```

```python
import jax
import jax.numpy as jnp
from jax import lax
from jax.sharding import PartitionSpec as P
from jax.experimental import pallas as pl
from jax.experimental.pallas import tpu as pltpu

D = 1600
FF = 6400
STEP = 10


BETA_ONE = 0.9
BETA_TWO = 0.999
EPSILON = 1e-06
LEARN_RATE = 0.25
DECAY_MAT = 0.01


def adam_direction(gradient, master, first, second, decay):
    first_new = BETA_ONE * first + (1.0 - BETA_ONE) * gradient
    second_new = BETA_TWO * second + (1.0 - BETA_TWO) * gradient * gradient
    corr_one = 1.0 - BETA_ONE**STEP
    corr_two = 1.0 - BETA_TWO**STEP
    direction = first_new / corr_one / (jnp.sqrt(second_new / corr_two) + EPSILON) + decay * master
    return (first_new, second_new, direction)


def segment_masks(position, bounds):
    lower = jnp.array(bounds[:-1], dtype=jnp.int32)[:, None]
    upper = jnp.array(bounds[1:], dtype=jnp.int32)[:, None]
    return ((position[None, :] >= lower) & (position[None, :] < upper)).astype(jnp.float32)


def all_sum(x, axes):
    count = 1
    for axis in axes:
        count *= lax.axis_size(axis)
    copies = jnp.broadcast_to(x[None], (count,) + x.shape)
    return jnp.sum(lax.all_to_all(copies, axes, 0, 0, tiled=True), axis=0)


def regroup_kernel(owned_rows, owned_vec, rows_ref, vec_ref, out_ref):
    per_step = out_ref.shape[0]
    for j in range(per_step):
        out_ref[j, :owned_rows, :] = rows_ref[j * owned_rows : (j + 1) * owned_rows, :].astype(jnp.float32)
        out_ref[j, owned_rows:, :] = jnp.zeros((1, out_ref.shape[2]), jnp.float32)
    for step in range(2):
        @pl.when(pl.program_id(0) == step)
        def _():
            for j in range(per_step):
                owner = step * per_step + j
                out_ref[j, owned_rows:, :owned_vec] = vec_ref[:, owner * owned_vec : (owner + 1) * owned_vec].astype(jnp.float32)


def regroup(rows, vec, n_owners, owned_rows):
    columns = rows.shape[1]
    owned_vec = vec.shape[1] // n_owners
    per_step = 8
    assert n_owners == 2 * per_step
    return pl.pallas_call(
        lambda r, v, o: regroup_kernel(owned_rows, owned_vec, r, v, o),
        grid=(n_owners // per_step,),
        in_specs=[
            pl.BlockSpec((per_step * owned_rows, columns), lambda i: (i, 0)),
            pl.BlockSpec((1, vec.shape[1]), lambda i: (0, 0)),
        ],
        out_specs=pl.BlockSpec((per_step, owned_rows + 1, columns), lambda i: (i, 0, 0)),
        out_shape=jax.ShapeDtypeStruct((n_owners, owned_rows + 1, columns), jnp.float32),
        compiler_params=pltpu.CompilerParams(vmem_limit_bytes=48 * 1024 * 1024),
    )(rows, vec)


def ungroup_kernel(owned_rows, in_ref, out_ref, vec_ref):
    owned_vec = vec_ref.shape[2]
    for j in range(in_ref.shape[0]):
        out_ref[j * owned_rows : (j + 1) * owned_rows, :] = in_ref[j, :owned_rows, :]
        vec_ref[j] = in_ref[j, owned_rows:, :owned_vec]


def ungroup(gathered, owned_rows, owned_vec):
    n_owners, _, columns = gathered.shape
    per_step = 8
    assert n_owners % per_step == 0
    return pl.pallas_call(
        lambda i, o, v: ungroup_kernel(owned_rows, i, o, v),
        grid=(n_owners // per_step,),
        in_specs=[pl.BlockSpec((per_step, gathered.shape[1], columns), lambda i: (i, 0, 0))],
        out_specs=[
            pl.BlockSpec((per_step * owned_rows, columns), lambda i: (i, 0)),
            pl.BlockSpec((per_step, 1, owned_vec), lambda i: (i, 0, 0)),
        ],
        out_shape=[
            jax.ShapeDtypeStruct((n_owners * owned_rows, columns), gathered.dtype),
            jax.ShapeDtypeStruct((n_owners, 1, owned_vec), gathered.dtype),
        ],
        compiler_params=pltpu.CompilerParams(vmem_limit_bytes=48 * 1024 * 1024),
    )(gathered)


def local(grad_mat, grad_vec, master_mat, first_mat, second_mat, master_vec, first_vec, second_vec):
    n_dp = lax.axis_size("dp")
    tensor_count = lax.axis_size("tensor")
    section_rows = grad_mat.shape[2]
    columns = grad_mat.shape[3]
    vec_length = grad_vec.shape[1]
    state_shape = master_mat.shape
    vec_shape = master_vec.shape
    owned_rows = state_shape[3]
    owned_vec = vec_shape[1]
    assert owned_vec <= columns and owned_rows * n_dp == section_rows
    master = master_mat.reshape(owned_rows, columns)
    master_v = master_vec.reshape(owned_vec)
    bounds_mat = [
        0,
        3 * D // tensor_count,
        4 * D // tensor_count,
        (4 * D + FF) // tensor_count,
        columns,
    ]
    masks_mat = segment_masks(lax.iota(jnp.int32, columns), bounds_mat)
    bounds_vec = [0, D, 2 * D, 5 * D, 6 * D, 7 * D, 8 * D, 8 * D + FF, 9 * D + FF]
    vec_index = lax.axis_index("dp") * owned_vec + lax.iota(jnp.int32, owned_vec)
    masks_vec = segment_masks(vec_index, bounds_vec)

    payload = regroup(grad_mat.reshape(section_rows, columns), grad_vec, n_dp, owned_rows)
    summed = lax.optimization_barrier(lax.psum_scatter(payload, "dp", scatter_dimension=0, tiled=True))
    gradient = summed[0, :owned_rows]
    gradient_v = summed[0, owned_rows, :owned_vec]

    first_new, second_new, direction = adam_direction(
        gradient, master, first_mat.reshape(owned_rows, columns), second_mat.reshape(owned_rows, columns), DECAY_MAT
    )
    first_v, second_v, direction_v = adam_direction(
        gradient_v, master_v, first_vec.reshape(owned_vec), second_vec.reshape(owned_vec), 0.0
    )
    weight_mat_sq = jnp.sum(masks_mat * jnp.sum(master * master, axis=0)[None, :], axis=1)
    weight_vec_sq = jnp.sum(masks_vec * (master_v * master_v)[None, :], axis=1)
    update_mat_sq = jnp.sum(masks_mat * jnp.sum(direction * direction, axis=0)[None, :], axis=1)
    update_vec_sq = jnp.sum(masks_vec * (direction_v * direction_v)[None, :], axis=1)

    vec_owner = (lax.axis_index("tensor") == 0) & (lax.axis_index("section") == 0)
    vec_part = jnp.where(vec_owner, jnp.concatenate([weight_vec_sq, update_vec_sq]), 0.0)
    sums = all_sum(jnp.concatenate([weight_mat_sq, update_mat_sq, vec_part]), ("dp", "tensor", "section"))
    n_mat = weight_mat_sq.shape[0]
    n_vec = weight_vec_sq.shape[0]
    wsum_mat, usum_mat = sums[:n_mat], sums[n_mat : 2 * n_mat]
    wsum_vec, usum_vec = sums[2 * n_mat : 2 * n_mat + n_vec], sums[2 * n_mat + n_vec :]
    ratio_mat = jnp.sqrt(wsum_mat) / jnp.sqrt(usum_mat)
    ratio_vec = jnp.sqrt(wsum_vec) / jnp.sqrt(usum_vec)
    ratio_cols = jnp.sum(masks_mat * ratio_mat[:, None], axis=0)
    ratio_entries = jnp.sum(masks_vec * ratio_vec[:, None], axis=0)
    master_new = master - LEARN_RATE * ratio_cols[None, :] * direction
    master_v_new = master_v - LEARN_RATE * ratio_entries * direction_v

    weights_v_row = jnp.pad(master_v_new.astype(jnp.bfloat16), (0, columns - owned_vec))[None, :]
    weights_rows = jnp.concatenate([master_new.astype(jnp.bfloat16), weights_v_row], axis=0)
    gathered = lax.all_gather(weights_rows, "dp", axis=0, tiled=False)
    weights_rows, weights_v_rows = ungroup(gathered, owned_rows, owned_vec)
    weights_mat = weights_rows.reshape(1, section_rows, columns)
    weights_vec = weights_v_rows.reshape(vec_length)
    return (
        weights_mat,
        weights_vec,
        master_new.reshape(state_shape),
        first_new.reshape(state_shape),
        second_new.reshape(state_shape),
        master_v_new.reshape(vec_shape),
        first_v.reshape(vec_shape),
        second_v.reshape(vec_shape),
    )


def solution(mesh):
    in_specs = (
        P("dp", "tensor", "section", None),
        P("dp", None),
        P("tensor", "section", "dp", None, None),
        P("tensor", "section", "dp", None, None),
        P("tensor", "section", "dp", None, None),
        P("dp", None),
        P("dp", None),
        P("dp", None),
    )
    out_specs = (
        P("tensor", "section", None),
        P(),
        P("tensor", "section", "dp", None, None),
        P("tensor", "section", "dp", None, None),
        P("tensor", "section", "dp", None, None),
        P("dp", None),
        P("dp", None),
        P("dp", None),
    )
    return jax.shard_map(local, mesh=mesh, in_specs=in_specs, out_specs=out_specs, check_vma=False)
```
